256 devices in a mesh: rows: 8 (over y, core), cols: 8 (over z), layers: 4 (over x).
Axes of the slice: x: 4, y: 4, z: 8, core: 2. Of those that a mesh axis runs over, the one named last changes fastest.
Arguments:
- y_blocks: bfloat16 [192, 32, 128, 128], P('rows', ('cols', 'layers')), may hold values from -1 to 1
- y_cols: int32 [192, 32], P('rows', ('cols', 'layers')), may hold values from 0 to 191, as said below
- prod_blocks: bfloat16 [192, 32, 128, 128], P('rows', ('cols', 'layers')), may hold values from -1 to 1
- prod_cols: int32 [192, 32], P('rows', ('cols', 'layers')), may hold values from 0 to 191, as said below
- out_cols: int32 [192, 32, 2], P('rows', ('cols', 'layers')), may hold values from 0 to 191, as said below
Outputs:
- y_next: bfloat16 [192, 32, 2, 128, 128], P('rows', ('cols', 'layers'))
The draws below stay inside these ranges and needn't reach their ends.
Inputs may be any that keep to these rules, and one draw needn't show every extreme that they name: y_cols[i, t] lies in [t * 6, (t + 1) * 6): each block row of Y holds exactly one block in each range of 6 block columns. prod_cols[k, t] lies in [t * 6, (t + 1) * 6): each block row of M holds exactly one block in each range of 6 block columns. out_cols[i, t, :] are 2 distinct block columns in [t * 6, (t + 1) * 6), one of them equal to y_cols[i, t].
All inputs are finite; a program needn't handle non-finite values.
Results may differ from the reference program's by a relative error of at most 0.001.
Values may be sent and summed in bfloat16 or wider, within the bound.
No kernel may reach another device: no remote copies, remote signals or barrier semaphores. Data moves between devices by JAX's collectives and lax.ppermute only.
A program may use at most 128 MiB of HBM per device.

```python
import jax
import jax.numpy as jnp
from jax import lax

BS = 128
TILE_COLS = 6
OUT_PER_TILE = 2
TILES = 32
NB = 192


def column_offsets(key):
    return jax.random.randint(jax.random.fold_in(key, 11), (NB, TILES), 0, TILE_COLS, dtype=jnp.int32)


def tile_starts():
    return (jnp.arange(TILES, dtype=jnp.int32) * TILE_COLS)[None, :]


def draw_y_cols(key, part):
    return tile_starts() + column_offsets(key)


def draw_prod_cols(key, part):
    offsets = jax.random.randint(jax.random.fold_in(key, 23), (NB, TILES), 0, TILE_COLS, dtype=jnp.int32)
    return tile_starts() + offsets


def draw_out_cols(key, part):
    y_offsets = column_offsets(key)
    candidates = jnp.arange(TILE_COLS, dtype=jnp.int32)
    scores = jax.random.randint(jax.random.fold_in(key, 37), (NB, TILES, TILE_COLS), 0, 1 << 20, dtype=jnp.int32)
    scores = scores * TILE_COLS + candidates[None, None, :]
    scores = jnp.where(candidates[None, None, :] == y_offsets[:, :, None], -1, scores)
    chosen = jnp.argsort(scores, axis=-1, stable=True)[:, :, :OUT_PER_TILE].astype(jnp.int32)
    rotation = jax.random.randint(jax.random.fold_in(key, 41), (NB, TILES, 1), 0, OUT_PER_TILE, dtype=jnp.int32)
    positions = (jnp.arange(OUT_PER_TILE, dtype=jnp.int32)[None, None, :] + rotation) % OUT_PER_TILE
    chosen = jnp.take_along_axis(chosen, positions, axis=-1)
    return tile_starts()[:, :, None] + chosen


def level_of(stream_key, shape, cuts, least, high):
    def one(axis_at, parts):
        draws = jax.random.uniform(jax.random.fold_in(jax.random.fold_in(stream_key, 6), axis_at), (parts,), jnp.float32, least / len(cuts), high / len(cuts))
        return jnp.repeat(jnp.exp(draws), shape[axis_at] // parts).reshape((-1,) + (1,) * (len(shape) - axis_at - 1))

    loudness = one(*cuts[0])
    for cut in cuts[1:]:
        loudness = loudness * one(*cut)
    return loudness


def noise(key, dims, scale, most, pieces=(), held_as=jnp.bfloat16):
    entries = jax.random.normal(key, dims, jnp.float32) * scale
    if len(pieces) > 0:
        entries = level_of(key, dims, pieces, -0.22, 0.18) * entries
    return jnp.clip(entries, min=-most, max=most).astype(held_as)


def setup_inputs(seed: int = 0) -> dict:
    keys = jax.random.split(jax.random.key(seed), 6)
    y_blocks = noise(keys[0], (NB, TILES, BS, BS), 0.18, 1.0, ((0, 8), (1, 32)))
    y_cols = draw_y_cols(jax.random.fold_in(keys[5], 71), 0)
    prod_blocks = noise(keys[2], (NB, TILES, BS, BS), 0.18, 1.0, ((0, 8), (1, 32)))
    prod_cols = draw_prod_cols(jax.random.fold_in(keys[5], 71), 0)
    out_cols = draw_out_cols(jax.random.fold_in(keys[5], 71), 0)
    return dict(y_blocks=y_blocks, y_cols=y_cols, prod_blocks=prod_blocks, prod_cols=prod_cols, out_cols=out_cols)


def reference(y_blocks, y_cols, prod_blocks, prod_cols, out_cols):
    def one_row(block_row):
        left_blocks = y_blocks[block_row].astype(jnp.float32)
        inner_cols = y_cols[block_row]
        right_blocks = prod_blocks[inner_cols].astype(jnp.float32)
        right_cols = prod_cols[inner_cols]
        target_cols = out_cols[block_row]
        present = (right_cols[:, :, None] == target_cols[None, :, :]).astype(jnp.float32)
        products = jnp.einsum("mab,mtbc->mtac", left_blocks, right_blocks)
        summed = jnp.einsum("mtw,mtac->twac", present, products)
        matches = (y_cols[block_row][:, None] == target_cols).astype(jnp.float32)
        updated = 1.5 * matches[:, :, None, None] * left_blocks[:, None] - 0.5 * summed
        return updated.astype(jnp.bfloat16)

    return lax.map(one_row, jnp.arange(NB, dtype=jnp.int32))
```

```python
import jax
import jax.numpy as jnp
from jax import lax
from jax.experimental import pallas as pl
from jax.experimental.pallas import tpu as pltpu
from jax.sharding import PartitionSpec as P


def _row_kernel(krow_ref, m0_ref, m1_ref, own_ref, y_ref, self_ref, lookup_ref, out_ref):
    i = pl.program_id(0)
    tiles = y_ref.shape[0]
    block = y_ref.shape[-1]

    def body(tp, carry):
        a0, a1 = carry
        at = i * tiles + tp
        k = krow_ref[at]
        p = jnp.dot(y_ref[tp, 0], lookup_ref[k], preferred_element_type=jnp.float32)
        a0 = a0 + jnp.where(m0_ref[at] != 0, p, 0.0)
        a1 = a1 + jnp.where(m1_ref[at] != 0, p, 0.0)
        return a0, a1

    zero = jnp.zeros((block, block), jnp.float32)
    a0, a1 = lax.fori_loop(0, tiles, body, (zero, zero))
    own = self_ref[0].astype(jnp.float32)
    own0 = jnp.where(own_ref[2 * i] != 0, own, 0.0)
    own1 = jnp.where(own_ref[2 * i + 1] != 0, own, 0.0)
    out_ref[0, 0] = (1.5 * own0 - 0.5 * a0).astype(out_ref.dtype)
    out_ref[0, 1] = (1.5 * own1 - 0.5 * a1).astype(out_ref.dtype)


def shards(y_blocks, y_cols, prod_blocks, prod_cols, out_cols):
    block_rows = y_blocks.shape[0]
    block_size = y_blocks.shape[2]
    out_width = out_cols.shape[2]

    lookup = lax.all_gather(prod_blocks[:, 0], "rows", axis=0, tiled=True)
    lookup_cols = lax.all_gather(prod_cols[:, 0], "rows", axis=0, tiled=True)
    left = lax.all_gather(y_blocks[:, 0], ("cols", "layers"), axis=0, tiled=False)
    left_cols = lax.all_gather(y_cols[:, 0], ("cols", "layers"), axis=0, tiled=False).T
    tiles = left.shape[0]

    krow = left_cols
    right_cols = lookup_cols[krow]
    m0 = (right_cols == out_cols[:, 0, 0][:, None]).astype(jnp.int32).reshape(-1)
    m1 = (right_cols == out_cols[:, 0, 1][:, None]).astype(jnp.int32).reshape(-1)
    own = (out_cols[:, 0, :] == y_cols[:, 0][:, None]).astype(jnp.int32).reshape(-1)

    nb = lookup.shape[0]
    out = pl.pallas_call(
        _row_kernel,
        out_shape=jax.ShapeDtypeStruct((block_rows, out_width, block_size, block_size), jnp.bfloat16),
        grid_spec=pltpu.PrefetchScalarGridSpec(
            num_scalar_prefetch=4,
            grid=(block_rows,),
            in_specs=[
                pl.BlockSpec((tiles, 1, block_size, block_size), lambda i, *_: (0, i, 0, 0)),
                pl.BlockSpec((1, block_size, block_size), lambda i, *_: (i, 0, 0)),
                pl.BlockSpec((nb, block_size, block_size), lambda i, *_: (0, 0, 0)),
            ],
            out_specs=pl.BlockSpec((1, out_width, block_size, block_size), lambda i, *_: (i, 0, 0, 0)),
        ),
        compiler_params=pltpu.CompilerParams(
            dimension_semantics=("arbitrary",),
            vmem_limit_bytes=40 * 1024 * 1024,
        ),
    )(krow.reshape(-1).astype(jnp.int32), m0, m1, own, left, y_blocks[:, 0], lookup)
    return out[:, None]


def solution(mesh):
    placed = (
        P("rows", ("cols", "layers"), None, None),
        P("rows", ("cols", "layers")),
        P("rows", ("cols", "layers"), None, None),
        P("rows", ("cols", "layers")),
        P("rows", ("cols", "layers"), None),
    )
    return jax.shard_map(
        shards,
        mesh=mesh,
        in_specs=placed,
        out_specs=P("rows", ("cols", "layers"), None, None, None),
        check_vma=False,
    )
```

```python
import jax
import jax.numpy as jnp
from jax import lax
from jax.experimental import pallas as pl
from jax.experimental.pallas import tpu as pltpu
from jax.sharding import PartitionSpec as P


def _row_kernel(krow_ref, m0_ref, m1_ref, own_ref, y_ref, self_ref, lookup_ref, out_ref, lhs_ref, stk_ref):
    i = pl.program_id(0)
    tiles = y_ref.shape[0]
    bs = y_ref.shape[-1]
    zeros = jnp.zeros((bs, bs), lhs_ref.dtype)
    for tp in range(tiles):
        at = i * tiles + tp
        cols = slice(tp * bs, (tp + 1) * bs)
        stk_ref[cols, :] = lookup_ref[krow_ref[at]]
        for w, m_ref in ((0, m0_ref), (1, m1_ref)):
            rows = slice(w * bs, (w + 1) * bs)
            hit = m_ref[at] != 0

            @pl.when(hit)
            def _():
                lhs_ref[rows, cols] = y_ref[tp, 0]

            @pl.when(jnp.logical_not(hit))
            def _():
                lhs_ref[rows, cols] = zeros

    res = jnp.dot(lhs_ref[...], stk_ref[...], preferred_element_type=jnp.float32)
    own = self_ref[0].astype(jnp.float32)
    for w in range(2):
        own_w = jnp.where(own_ref[2 * i + w] != 0, own, 0.0)
        out_ref[0, w] = (1.5 * own_w - 0.5 * res[w * bs:(w + 1) * bs]).astype(out_ref.dtype)


def shards(y_blocks, y_cols, prod_blocks, prod_cols, out_cols):
    block_rows = y_blocks.shape[0]
    block_size = y_blocks.shape[2]
    out_width = out_cols.shape[2]

    lookup = lax.all_gather(prod_blocks[:, 0], "rows", axis=0, tiled=True)
    lookup_cols = lax.all_gather(prod_cols[:, 0], "rows", axis=0, tiled=True)
    left = lax.all_gather(y_blocks[:, 0], ("cols", "layers"), axis=0, tiled=False)
    left_cols = lax.all_gather(y_cols[:, 0], ("cols", "layers"), axis=0, tiled=False).T
    tiles = left.shape[0]

    krow = left_cols
    right_cols = lookup_cols[krow]
    m0 = (right_cols == out_cols[:, 0, 0][:, None]).astype(jnp.int32).reshape(-1)
    m1 = (right_cols == out_cols[:, 0, 1][:, None]).astype(jnp.int32).reshape(-1)
    own = (out_cols[:, 0, :] == y_cols[:, 0][:, None]).astype(jnp.int32).reshape(-1)

    nb = lookup.shape[0]
    out = pl.pallas_call(
        _row_kernel,
        out_shape=jax.ShapeDtypeStruct((block_rows, out_width, block_size, block_size), jnp.bfloat16),
        grid_spec=pltpu.PrefetchScalarGridSpec(
            num_scalar_prefetch=4,
            grid=(block_rows,),
            in_specs=[
                pl.BlockSpec((tiles, 1, block_size, block_size), lambda i, *_: (0, i, 0, 0)),
                pl.BlockSpec((1, block_size, block_size), lambda i, *_: (i, 0, 0)),
                pl.BlockSpec((nb, block_size, block_size), lambda i, *_: (0, 0, 0)),
            ],
            out_specs=pl.BlockSpec((1, out_width, block_size, block_size), lambda i, *_: (i, 0, 0, 0)),
            scratch_shapes=[
                pltpu.VMEM((out_width * block_size, tiles * block_size), jnp.bfloat16),
                pltpu.VMEM((tiles * block_size, block_size), jnp.bfloat16),
            ],
        ),
        compiler_params=pltpu.CompilerParams(
            dimension_semantics=("arbitrary",),
            vmem_limit_bytes=40 * 1024 * 1024,
        ),
    )(krow.reshape(-1).astype(jnp.int32), m0, m1, own, left, y_blocks[:, 0], lookup)
    return out[:, None]


def solution(mesh):
    placed = (
        P("rows", ("cols", "layers"), None, None),
        P("rows", ("cols", "layers")),
        P("rows", ("cols", "layers"), None, None),
        P("rows", ("cols", "layers")),
        P("rows", ("cols", "layers"), None),
    )
    return jax.shard_map(
        shards,
        mesh=mesh,
        in_specs=placed,
        out_specs=P("rows", ("cols", "layers"), None, None, None),
        check_vma=False,
    )
```

```python
import jax
import jax.numpy as jnp
from jax import lax
from jax.experimental import pallas as pl
from jax.experimental.pallas import tpu as pltpu
from jax.sharding import PartitionSpec as P


def _row_kernel(krow_ref, m0_ref, m1_ref, own_ref, y_ref, self_ref, lookup_ref, out_ref, lhs_ref, stk_ref):
    i = pl.program_id(0)
    tiles = y_ref.shape[0]
    bs = y_ref.shape[-1]
    zeros = jnp.zeros((bs, bs), lhs_ref.dtype)
    for tp in range(tiles):
        at = i * tiles + tp
        cols = slice(tp * bs, (tp + 1) * bs)
        stk_ref[cols, :] = lookup_ref[krow_ref[at]]
        for w, m_ref in ((0, m0_ref), (1, m1_ref)):
            rows = slice(w * bs, (w + 1) * bs)
            hit = m_ref[at] != 0

            @pl.when(hit)
            def _():
                lhs_ref[rows, cols] = y_ref[tp, 0]

            @pl.when(jnp.logical_not(hit))
            def _():
                lhs_ref[rows, cols] = zeros

    res = jnp.dot(lhs_ref[...], stk_ref[...], preferred_element_type=jnp.float32)
    own = self_ref[0].astype(jnp.float32)
    for w in range(2):
        own_w = jnp.where(own_ref[2 * i + w] != 0, own, 0.0)
        out_ref[0, w] = (1.5 * own_w - 0.5 * res[w * bs:(w + 1) * bs]).astype(out_ref.dtype)


def shards(y_blocks, y_cols, prod_blocks, prod_cols, out_cols):
    block_rows = y_blocks.shape[0]
    block_size = y_blocks.shape[2]
    out_width = out_cols.shape[2]

    groups = lax.axis_size("rows")
    me = lax.axis_index("rows")
    pieces = [prod_blocks[:, 0]]
    for s in range(1, groups):
        pieces.append(lax.ppermute(prod_blocks[:, 0], "rows", [(r, (r + s) % groups) for r in range(groups)]))
    lookup = jnp.concatenate(pieces, axis=0)
    lookup_cols = lax.all_gather(prod_cols[:, 0], "rows", axis=0, tiled=True)
    left = lax.all_gather(y_blocks[:, 0], ("cols", "layers"), axis=0, tiled=False)
    left_cols = lax.all_gather(y_cols[:, 0], ("cols", "layers"), axis=0, tiled=False).T
    tiles = left.shape[0]

    right_cols = lookup_cols[left_cols]
    owner = left_cols // block_rows
    krow = ((me - owner) % groups) * block_rows + left_cols % block_rows
    m0 = (right_cols == out_cols[:, 0, 0][:, None]).astype(jnp.int32).reshape(-1)
    m1 = (right_cols == out_cols[:, 0, 1][:, None]).astype(jnp.int32).reshape(-1)
    own = (out_cols[:, 0, :] == y_cols[:, 0][:, None]).astype(jnp.int32).reshape(-1)

    nb = lookup.shape[0]
    out = pl.pallas_call(
        _row_kernel,
        out_shape=jax.ShapeDtypeStruct((block_rows, out_width, block_size, block_size), jnp.bfloat16),
        grid_spec=pltpu.PrefetchScalarGridSpec(
            num_scalar_prefetch=4,
            grid=(block_rows,),
            in_specs=[
                pl.BlockSpec((tiles, 1, block_size, block_size), lambda i, *_: (0, i, 0, 0)),
                pl.BlockSpec((1, block_size, block_size), lambda i, *_: (i, 0, 0)),
                pl.BlockSpec((nb, block_size, block_size), lambda i, *_: (0, 0, 0)),
            ],
            out_specs=pl.BlockSpec((1, out_width, block_size, block_size), lambda i, *_: (i, 0, 0, 0)),
            scratch_shapes=[
                pltpu.VMEM((out_width * block_size, tiles * block_size), jnp.bfloat16),
                pltpu.VMEM((tiles * block_size, block_size), jnp.bfloat16),
            ],
        ),
        compiler_params=pltpu.CompilerParams(
            dimension_semantics=("arbitrary",),
            vmem_limit_bytes=40 * 1024 * 1024,
        ),
    )(krow.reshape(-1).astype(jnp.int32), m0, m1, own, left, y_blocks[:, 0], lookup)
    return out[:, None]


def solution(mesh):
    placed = (
        P("rows", ("cols", "layers"), None, None),
        P("rows", ("cols", "layers")),
        P("rows", ("cols", "layers"), None, None),
        P("rows", ("cols", "layers")),
        P("rows", ("cols", "layers"), None),
    )
    return jax.shard_map(
        shards,
        mesh=mesh,
        in_specs=placed,
        out_specs=P("rows", ("cols", "layers"), None, None, None),
        check_vma=False,
    )
```

```python
import jax
import jax.numpy as jnp
from jax import lax
from jax.experimental import pallas as pl
from jax.experimental.pallas import tpu as pltpu
from jax.sharding import PartitionSpec as P


CHUNKS = 4


def _row_kernel(i0_ref, i1_ref, own_ref, y_ref, self_ref, lookup_ref, out_ref, lhs_ref, stk_ref):
    i = pl.program_id(0)
    tiles = y_ref.shape[0]
    bs = y_ref.shape[-1]
    for tp in range(tiles):
        at = i * tiles + tp
        cols = slice(tp * bs, (tp + 1) * bs)
        lhs_ref[:, cols] = y_ref[tp, 0]
        stk_ref[cols, 0:bs] = lookup_ref[i0_ref[at]]
        stk_ref[cols, bs:2 * bs] = lookup_ref[i1_ref[at]]
    res = jnp.dot(lhs_ref[...], stk_ref[...], preferred_element_type=jnp.float32)
    own = self_ref[0].astype(jnp.float32)
    for w in range(2):
        own_w = jnp.where(own_ref[2 * i + w] != 0, own, 0.0)
        out_ref[0, w] = (1.5 * own_w - 0.5 * res[:, w * bs:(w + 1) * bs]).astype(out_ref.dtype)


def _rows_product(i0, i1, own, left, own_blocks, lookup, out_width):
    tiles, block_rows, block_size, _ = left.shape
    nb = lookup.shape[0]
    return pl.pallas_call(
        _row_kernel,
        out_shape=jax.ShapeDtypeStruct((block_rows, out_width, block_size, block_size), jnp.bfloat16),
        grid_spec=pltpu.PrefetchScalarGridSpec(
            num_scalar_prefetch=3,
            grid=(block_rows,),
            in_specs=[
                pl.BlockSpec((tiles, 1, block_size, block_size), lambda i, *_: (0, i, 0, 0)),
                pl.BlockSpec((1, block_size, block_size), lambda i, *_: (i, 0, 0)),
                pl.BlockSpec((nb, block_size, block_size), lambda i, *_: (0, 0, 0)),
            ],
            out_specs=pl.BlockSpec((1, out_width, block_size, block_size), lambda i, *_: (i, 0, 0, 0)),
            scratch_shapes=[
                pltpu.VMEM((block_size, tiles * block_size), jnp.bfloat16),
                pltpu.VMEM((tiles * block_size, out_width * block_size), jnp.bfloat16),
            ],
        ),
        compiler_params=pltpu.CompilerParams(
            dimension_semantics=("arbitrary",),
            vmem_limit_bytes=40 * 1024 * 1024,
        ),
    )(i0, i1, own, left, own_blocks, lookup)


def shards(y_blocks, y_cols, prod_blocks, prod_cols, out_cols):
    block_rows = y_blocks.shape[0]
    block_size = y_blocks.shape[2]
    out_width = out_cols.shape[2]

    groups = lax.axis_size("rows")
    me = lax.axis_index("rows")
    pieces = [prod_blocks[:, 0]]
    for s in range(1, groups):
        pieces.append(lax.ppermute(prod_blocks[:, 0], "rows", [(r, (r + s) % groups) for r in range(groups)]))
    pieces.append(jnp.zeros((1, block_size, block_size), prod_blocks.dtype))
    lookup = jnp.concatenate(pieces, axis=0)
    nb = groups * block_rows
    lookup_cols = lax.all_gather(prod_cols[:, 0], "rows", axis=0, tiled=True)
    left_cols = lax.all_gather(y_cols[:, 0], ("cols", "layers"), axis=0, tiled=False).T

    right_cols = lookup_cols[left_cols]
    owner = left_cols // block_rows
    krow = ((me - owner) % groups) * block_rows + left_cols % block_rows
    i0 = jnp.where(right_cols == out_cols[:, 0, 0][:, None], krow, nb).astype(jnp.int32)
    i1 = jnp.where(right_cols == out_cols[:, 0, 1][:, None], krow, nb).astype(jnp.int32)
    own = (out_cols[:, 0, :] == y_cols[:, 0][:, None]).astype(jnp.int32)

    step = block_rows // CHUNKS
    outs = []
    for c in range(CHUNKS):
        rows = slice(c * step, (c + 1) * step)
        left = lax.all_gather(y_blocks[rows, 0], ("cols", "layers"), axis=0, tiled=False)
        outs.append(_rows_product(
            i0[rows].reshape(-1), i1[rows].reshape(-1), own[rows].reshape(-1),
            left, y_blocks[rows, 0], lookup, out_width))
    return jnp.concatenate(outs, axis=0)[:, None]


def solution(mesh):
    placed = (
        P("rows", ("cols", "layers"), None, None),
        P("rows", ("cols", "layers")),
        P("rows", ("cols", "layers"), None, None),
        P("rows", ("cols", "layers")),
        P("rows", ("cols", "layers"), None),
    )
    return jax.shard_map(
        shards,
        mesh=mesh,
        in_specs=placed,
        out_specs=P("rows", ("cols", "layers"), None, None, None),
        check_vma=False,
    )
```

```python
import jax
import jax.numpy as jnp
from jax import lax
from jax.experimental import pallas as pl
from jax.experimental.pallas import tpu as pltpu
from jax.sharding import PartitionSpec as P


CHUNKS = 1


def _row_kernel(i0_ref, i1_ref, own_ref, y_ref, self_ref, lookup_ref, out_ref, lhs_ref, stk_ref):
    i = pl.program_id(0)
    tiles = y_ref.shape[0]
    bs = y_ref.shape[-1]
    for tp in range(tiles):
        at = i * tiles + tp
        cols = slice(tp * bs, (tp + 1) * bs)
        lhs_ref[:, cols] = y_ref[tp, 0]
        stk_ref[cols, 0:bs] = lookup_ref[i0_ref[at]]
        stk_ref[cols, bs:2 * bs] = lookup_ref[i1_ref[at]]
    res = jnp.dot(lhs_ref[...], stk_ref[...], preferred_element_type=jnp.float32)
    own = self_ref[0].astype(jnp.float32)
    for w in range(2):
        own_w = jnp.where(own_ref[2 * i + w] != 0, own, 0.0)
        out_ref[0, w] = (1.5 * own_w - 0.5 * res[:, w * bs:(w + 1) * bs]).astype(out_ref.dtype)


def _rows_product(i0, i1, own, left, own_blocks, lookup, out_width):
    tiles, block_rows, block_size, _ = left.shape
    nb = lookup.shape[0]
    return pl.pallas_call(
        _row_kernel,
        out_shape=jax.ShapeDtypeStruct((block_rows, out_width, block_size, block_size), jnp.bfloat16),
        grid_spec=pltpu.PrefetchScalarGridSpec(
            num_scalar_prefetch=3,
            grid=(block_rows,),
            in_specs=[
                pl.BlockSpec((tiles, 1, block_size, block_size), lambda i, *_: (0, i, 0, 0)),
                pl.BlockSpec((1, block_size, block_size), lambda i, *_: (i, 0, 0)),
                pl.BlockSpec((nb, block_size, block_size), lambda i, *_: (0, 0, 0)),
            ],
            out_specs=pl.BlockSpec((1, out_width, block_size, block_size), lambda i, *_: (i, 0, 0, 0)),
            scratch_shapes=[
                pltpu.VMEM((block_size, tiles * block_size), jnp.bfloat16),
                pltpu.VMEM((tiles * block_size, out_width * block_size), jnp.bfloat16),
            ],
        ),
        compiler_params=pltpu.CompilerParams(
            dimension_semantics=("arbitrary",),
            vmem_limit_bytes=40 * 1024 * 1024,
        ),
    )(i0, i1, own, left, own_blocks, lookup)


def shards(y_blocks, y_cols, prod_blocks, prod_cols, out_cols):
    block_rows = y_blocks.shape[0]
    block_size = y_blocks.shape[2]
    out_width = out_cols.shape[2]

    groups = lax.axis_size("rows")
    me = lax.axis_index("rows")
    pieces = [prod_blocks[:, 0]]
    for s in range(1, groups):
        pieces.append(lax.ppermute(prod_blocks[:, 0], "rows", [(r, (r + s) % groups) for r in range(groups)]))
    pieces.append(jnp.zeros((1, block_size, block_size), prod_blocks.dtype))
    lookup = jnp.concatenate(pieces, axis=0)
    nb = groups * block_rows
    lookup_cols = lax.all_gather(prod_cols[:, 0], "rows", axis=0, tiled=True)
    left_cols = lax.all_gather(y_cols[:, 0], ("cols", "layers"), axis=0, tiled=False).T

    right_cols = lookup_cols[left_cols]
    owner = left_cols // block_rows
    krow = ((me - owner) % groups) * block_rows + left_cols % block_rows
    i0 = jnp.where(right_cols == out_cols[:, 0, 0][:, None], krow, nb).astype(jnp.int32)
    i1 = jnp.where(right_cols == out_cols[:, 0, 1][:, None], krow, nb).astype(jnp.int32)
    own = (out_cols[:, 0, :] == y_cols[:, 0][:, None]).astype(jnp.int32)

    step = block_rows // CHUNKS
    outs = []
    for c in range(CHUNKS):
        rows = slice(c * step, (c + 1) * step)
        left = lax.all_gather(y_blocks[rows, 0], ("cols", "layers"), axis=0, tiled=False)
        outs.append(_rows_product(
            i0[rows].reshape(-1), i1[rows].reshape(-1), own[rows].reshape(-1),
            left, y_blocks[rows, 0], lookup, out_width))
    return jnp.concatenate(outs, axis=0)[:, None]


def solution(mesh):
    placed = (
        P("rows", ("cols", "layers"), None, None),
        P("rows", ("cols", "layers")),
        P("rows", ("cols", "layers"), None, None),
        P("rows", ("cols", "layers")),
        P("rows", ("cols", "layers"), None),
    )
    return jax.shard_map(
        shards,
        mesh=mesh,
        in_specs=placed,
        out_specs=P("rows", ("cols", "layers"), None, None, None),
        check_vma=False,
    )
```

```python
import jax
import jax.numpy as jnp
from jax import lax
from jax.experimental import pallas as pl
from jax.experimental.pallas import tpu as pltpu
from jax.sharding import PartitionSpec as P


def _stack_kernel(krow_ref, lookup_ref, out_ref):
    i = pl.program_id(0)
    tiles = out_ref.shape[1] // out_ref.shape[2]
    bs = out_ref.shape[2]
    for tp in range(tiles):
        out_ref[0, tp * bs:(tp + 1) * bs, :] = lookup_ref[krow_ref[i * tiles + tp]]


def _stack_rows(krow, lookup, block_rows, tiles):
    nb, bs, _ = lookup.shape
    return pl.pallas_call(
        _stack_kernel,
        out_shape=jax.ShapeDtypeStruct((block_rows, tiles * bs, bs), lookup.dtype),
        grid_spec=pltpu.PrefetchScalarGridSpec(
            num_scalar_prefetch=1,
            grid=(block_rows,),
            in_specs=[pl.BlockSpec((nb, bs, bs), lambda i, *_: (0, 0, 0))],
            out_specs=pl.BlockSpec((1, tiles * bs, bs), lambda i, *_: (i, 0, 0)),
        ),
        compiler_params=pltpu.CompilerParams(
            dimension_semantics=("arbitrary",),
            vmem_limit_bytes=40 * 1024 * 1024,
        ),
    )(krow, lookup)


def _row_kernel(m0_ref, m1_ref, own_ref, y_ref, self_ref, stk_ref, out_ref, lhs_ref):
    i = pl.program_id(0)
    tiles = y_ref.shape[0]
    bs = y_ref.shape[-1]
    for tp in range(tiles):
        at = i * tiles + tp
        cols = slice(tp * bs, (tp + 1) * bs)
        y = y_ref[tp, 0]
        zero = jnp.zeros_like(y)
        lhs_ref[0:bs, cols] = jnp.where(m0_ref[at] != 0, y, zero)
        lhs_ref[bs:2 * bs, cols] = jnp.where(m1_ref[at] != 0, y, zero)
    res = jnp.dot(lhs_ref[...], stk_ref[0], preferred_element_type=jnp.float32)
    own = self_ref[0].astype(jnp.float32)
    for w in range(2):
        own_w = jnp.where(own_ref[2 * i + w] != 0, own, 0.0)
        out_ref[0, w] = (1.5 * own_w - 0.5 * res[w * bs:(w + 1) * bs]).astype(out_ref.dtype)


def _rows_product(m0, m1, own, left, own_blocks, stacked, out_width):
    tiles, block_rows, block_size, _ = left.shape
    return pl.pallas_call(
        _row_kernel,
        out_shape=jax.ShapeDtypeStruct((block_rows, out_width, block_size, block_size), jnp.bfloat16),
        grid_spec=pltpu.PrefetchScalarGridSpec(
            num_scalar_prefetch=3,
            grid=(block_rows,),
            in_specs=[
                pl.BlockSpec((tiles, 1, block_size, block_size), lambda i, *_: (0, i, 0, 0)),
                pl.BlockSpec((1, block_size, block_size), lambda i, *_: (i, 0, 0)),
                pl.BlockSpec((1, tiles * block_size, block_size), lambda i, *_: (i, 0, 0)),
            ],
            out_specs=pl.BlockSpec((1, out_width, block_size, block_size), lambda i, *_: (i, 0, 0, 0)),
            scratch_shapes=[
                pltpu.VMEM((out_width * block_size, tiles * block_size), jnp.bfloat16),
            ],
        ),
        compiler_params=pltpu.CompilerParams(
            dimension_semantics=("arbitrary",),
            vmem_limit_bytes=40 * 1024 * 1024,
        ),
    )(m0, m1, own, left, own_blocks, stacked)


def shards(y_blocks, y_cols, prod_blocks, prod_cols, out_cols):
    block_rows = y_blocks.shape[0]
    block_size = y_blocks.shape[2]
    out_width = out_cols.shape[2]

    groups = lax.axis_size("rows")
    me = lax.axis_index("rows")
    pieces = [prod_blocks[:, 0]]
    for s in range(1, groups):
        pieces.append(lax.ppermute(prod_blocks[:, 0], "rows", [(r, (r + s) % groups) for r in range(groups)]))
    lookup = jnp.concatenate(pieces, axis=0)
    lookup_cols = lax.all_gather(prod_cols[:, 0], "rows", axis=0, tiled=True)
    left_cols = lax.all_gather(y_cols[:, 0], ("cols", "layers"), axis=0, tiled=False).T

    right_cols = lookup_cols[left_cols]
    owner = left_cols // block_rows
    krow = ((me - owner) % groups) * block_rows + left_cols % block_rows
    m0 = (right_cols == out_cols[:, 0, 0][:, None]).astype(jnp.int32)
    m1 = (right_cols == out_cols[:, 0, 1][:, None]).astype(jnp.int32)
    own = (out_cols[:, 0, :] == y_cols[:, 0][:, None]).astype(jnp.int32)

    tiles = left_cols.shape[1]
    stacked = _stack_rows(krow.reshape(-1).astype(jnp.int32), lookup, block_rows, tiles)

    left = lax.all_gather(y_blocks[:, 0], ("cols", "layers"), axis=0, tiled=False)
    out = _rows_product(m0.reshape(-1), m1.reshape(-1), own.reshape(-1), left, y_blocks[:, 0], stacked, out_width)
    return out[:, None]


def solution(mesh):
    placed = (
        P("rows", ("cols", "layers"), None, None),
        P("rows", ("cols", "layers")),
        P("rows", ("cols", "layers"), None, None),
        P("rows", ("cols", "layers")),
        P("rows", ("cols", "layers"), None),
    )
    return jax.shard_map(
        shards,
        mesh=mesh,
        in_specs=placed,
        out_specs=P("rows", ("cols", "layers"), None, None, None),
        check_vma=False,
    )
```

```python
import jax
import jax.numpy as jnp
from jax import lax
from jax.experimental import pallas as pl
from jax.experimental.pallas import tpu as pltpu
from jax.sharding import PartitionSpec as P


ROWS_PER_STEP = 4
SIDE_ROWS = 4


def _row_kernel(i0_ref, i1_ref, own_ref, y_ref, self_ref, lookup_ref, out_ref, lhs_ref, stk_ref):
    g = pl.program_id(0)
    tiles = y_ref.shape[0]
    rb = y_ref.shape[1]
    bs = y_ref.shape[-1]
    for r in range(rb):
        i = g * rb + r
        for tp in range(tiles):
            at = i * tiles + tp
            cols = slice(tp * bs, (tp + 1) * bs)
            lhs_ref[:, cols] = y_ref[tp, r]
            stk_ref[cols, 0:bs] = lookup_ref[i0_ref[at]]
            stk_ref[cols, bs:2 * bs] = lookup_ref[i1_ref[at]]
        res = jnp.dot(lhs_ref[...], stk_ref[...], preferred_element_type=jnp.float32)
        own = self_ref[r].astype(jnp.float32)
        for w in range(2):
            own_w = jnp.where(own_ref[2 * i + w] != 0, own, 0.0)
            out_ref[r, w] = (1.5 * own_w - 0.5 * res[:, w * bs:(w + 1) * bs]).astype(out_ref.dtype)


def _rows_product(i0, i1, own, left, own_blocks, lookup, out_width):
    tiles, block_rows, block_size, _ = left.shape
    nb = lookup.shape[0]
    rb = ROWS_PER_STEP if block_rows % ROWS_PER_STEP == 0 else 1
    return pl.pallas_call(
        _row_kernel,
        out_shape=jax.ShapeDtypeStruct((block_rows, out_width, block_size, block_size), jnp.bfloat16),
        grid_spec=pltpu.PrefetchScalarGridSpec(
            num_scalar_prefetch=3,
            grid=(block_rows // rb,),
            in_specs=[
                pl.BlockSpec((tiles, rb, block_size, block_size), lambda g, *_: (0, g, 0, 0)),
                pl.BlockSpec((rb, block_size, block_size), lambda g, *_: (g, 0, 0)),
                pl.BlockSpec((nb, block_size, block_size), lambda g, *_: (0, 0, 0)),
            ],
            out_specs=pl.BlockSpec((rb, out_width, block_size, block_size), lambda g, *_: (g, 0, 0, 0)),
            scratch_shapes=[
                pltpu.VMEM((block_size, tiles * block_size), jnp.bfloat16),
                pltpu.VMEM((tiles * block_size, out_width * block_size), jnp.bfloat16),
            ],
        ),
        compiler_params=pltpu.CompilerParams(
            dimension_semantics=("arbitrary",),
            vmem_limit_bytes=48 * 1024 * 1024,
        ),
    )(i0, i1, own, left, own_blocks, lookup)


def shards(y_blocks, y_cols, prod_blocks, prod_cols, out_cols):
    block_rows = y_blocks.shape[0]
    block_size = y_blocks.shape[2]
    out_width = out_cols.shape[2]

    groups = lax.axis_size("rows")
    me = lax.axis_index("rows")
    pieces = [prod_blocks[:, 0]]
    for s in range(1, groups):
        pieces.append(lax.ppermute(prod_blocks[:, 0], "rows", [(r, (r + s) % groups) for r in range(groups)]))
    pieces.append(jnp.zeros((1, block_size, block_size), prod_blocks.dtype))
    lookup = jnp.concatenate(pieces, axis=0)
    nb = groups * block_rows
    lookup_cols = lax.all_gather(prod_cols[:, 0], "rows", axis=0, tiled=True)
    left_cols = lax.all_gather(y_cols[:, 0], ("cols", "layers"), axis=0, tiled=False).T

    right_cols = lookup_cols[left_cols]
    owner = left_cols // block_rows
    krow = ((me - owner) % groups) * block_rows + left_cols % block_rows
    i0 = jnp.where(right_cols == out_cols[:, 0, 0][:, None], krow, nb).astype(jnp.int32)
    i1 = jnp.where(right_cols == out_cols[:, 0, 1][:, None], krow, nb).astype(jnp.int32)
    own = (out_cols[:, 0, :] == y_cols[:, 0][:, None]).astype(jnp.int32)

    tiles = left_cols.shape[1]
    main = block_rows - SIDE_ROWS
    side_rows = slice(main, block_rows)
    side = lax.all_to_all(
        jnp.tile(y_blocks[side_rows, 0], (tiles, 1, 1)), ("cols", "layers"), 0, 0, tiled=True)
    side = side.reshape(tiles, SIDE_ROWS, block_size, block_size)
    out_side = _rows_product(
        i0[side_rows].reshape(-1), i1[side_rows].reshape(-1), own[side_rows].reshape(-1),
        side, y_blocks[side_rows, 0], lookup, out_width)
    rows = slice(0, main)
    left = lax.all_gather(y_blocks[rows, 0], ("cols", "layers"), axis=0, tiled=False)
    out_main = _rows_product(
        i0[rows].reshape(-1), i1[rows].reshape(-1), own[rows].reshape(-1),
        left, y_blocks[rows, 0], lookup, out_width)
    return jnp.concatenate([out_main, out_side], axis=0)[:, None]


def solution(mesh):
    placed = (
        P("rows", ("cols", "layers"), None, None),
        P("rows", ("cols", "layers")),
        P("rows", ("cols", "layers"), None, None),
        P("rows", ("cols", "layers")),
        P("rows", ("cols", "layers"), None),
    )
    return jax.shard_map(
        shards,
        mesh=mesh,
        in_specs=placed,
        out_specs=P("rows", ("cols", "layers"), None, None, None),
        check_vma=False,
    )
```

```python
import jax
import jax.numpy as jnp
from jax import lax
from jax.experimental import pallas as pl
from jax.experimental.pallas import tpu as pltpu
from jax.sharding import PartitionSpec as P


ROWS_PER_STEP = 4


def _row_kernel(i0_ref, i1_ref, own_ref, y_ref, self_ref, lookup_ref, out_ref, lhs_ref, stk_ref):
    g = pl.program_id(0)
    tiles = y_ref.shape[0]
    rb = y_ref.shape[1]
    bs = y_ref.shape[-1]
    for r in range(rb):
        i = g * rb + r
        for tp in range(tiles):
            at = i * tiles + tp
            cols = slice(tp * bs, (tp + 1) * bs)
            lhs_ref[:, cols] = y_ref[tp, r]
            stk_ref[cols, 0:bs] = lookup_ref[i0_ref[at]]
            stk_ref[cols, bs:2 * bs] = lookup_ref[i1_ref[at]]
        res = jnp.dot(lhs_ref[...], stk_ref[...], preferred_element_type=jnp.float32)
        own = self_ref[r].astype(jnp.float32)
        for w in range(2):
            own_w = jnp.where(own_ref[2 * i + w] != 0, own, 0.0)
            out_ref[r, w] = (1.5 * own_w - 0.5 * res[:, w * bs:(w + 1) * bs]).astype(out_ref.dtype)


def _rows_product(i0, i1, own, left, own_blocks, lookup, out_width):
    tiles, block_rows, block_size, _ = left.shape
    nb = lookup.shape[0]
    rb = ROWS_PER_STEP if block_rows % ROWS_PER_STEP == 0 else 1
    return pl.pallas_call(
        _row_kernel,
        out_shape=jax.ShapeDtypeStruct((block_rows, out_width, block_size, block_size), jnp.bfloat16),
        grid_spec=pltpu.PrefetchScalarGridSpec(
            num_scalar_prefetch=3,
            grid=(block_rows // rb,),
            in_specs=[
                pl.BlockSpec((tiles, rb, block_size, block_size), lambda g, *_: (0, g, 0, 0)),
                pl.BlockSpec((rb, block_size, block_size), lambda g, *_: (g, 0, 0)),
                pl.BlockSpec((nb, block_size, block_size), lambda g, *_: (0, 0, 0)),
            ],
            out_specs=pl.BlockSpec((rb, out_width, block_size, block_size), lambda g, *_: (g, 0, 0, 0)),
            scratch_shapes=[
                pltpu.VMEM((block_size, tiles * block_size), jnp.bfloat16),
                pltpu.VMEM((tiles * block_size, out_width * block_size), jnp.bfloat16),
            ],
        ),
        compiler_params=pltpu.CompilerParams(
            dimension_semantics=("arbitrary",),
            vmem_limit_bytes=48 * 1024 * 1024,
        ),
    )(i0, i1, own, left, own_blocks, lookup)


def shards(y_blocks, y_cols, prod_blocks, prod_cols, out_cols):
    block_rows = y_blocks.shape[0]
    block_size = y_blocks.shape[2]
    out_width = out_cols.shape[2]

    groups = lax.axis_size("rows")
    me = lax.axis_index("rows")
    pieces = [prod_blocks[:, 0]]
    for s in range(1, groups):
        pieces.append(lax.ppermute(prod_blocks[:, 0], "rows", [(r, (r + s) % groups) for r in range(groups)]))
    pieces.append(jnp.zeros((1, block_size, block_size), prod_blocks.dtype))
    lookup = jnp.concatenate(pieces, axis=0)
    nb = groups * block_rows
    lookup_cols = lax.all_gather(prod_cols[:, 0], "rows", axis=0, tiled=True)
    left_cols = lax.all_gather(y_cols[:, 0], ("cols", "layers"), axis=0, tiled=False).T

    right_cols = lookup_cols[left_cols]
    owner = left_cols // block_rows
    krow = ((me - owner) % groups) * block_rows + left_cols % block_rows
    i0 = jnp.where(right_cols == out_cols[:, 0, 0][:, None], krow, nb).astype(jnp.int32)
    i1 = jnp.where(right_cols == out_cols[:, 0, 1][:, None], krow, nb).astype(jnp.int32)
    own = (out_cols[:, 0, :] == y_cols[:, 0][:, None]).astype(jnp.int32)

    left = lax.all_gather(y_blocks[:, 0], ("cols", "layers"), axis=0, tiled=False)
    out = _rows_product(
        i0.reshape(-1), i1.reshape(-1), own.reshape(-1), left, y_blocks[:, 0], lookup, out_width)
    return out[:, None]


def solution(mesh):
    placed = (
        P("rows", ("cols", "layers"), None, None),
        P("rows", ("cols", "layers")),
        P("rows", ("cols", "layers"), None, None),
        P("rows", ("cols", "layers")),
        P("rows", ("cols", "layers"), None),
    )
    return jax.shard_map(
        shards,
        mesh=mesh,
        in_specs=placed,
        out_specs=P("rows", ("cols", "layers"), None, None, None),
        check_vma=False,
    )
```

```python
import jax
import jax.numpy as jnp
from jax import lax
from jax.experimental import pallas as pl
from jax.experimental.pallas import tpu as pltpu
from jax.sharding import PartitionSpec as P


ROWS_PER_STEP = 4


def _row_kernel(i0_ref, i1_ref, own_ref, y_ref, self_ref, lookup_ref, out_ref, stk_ref):
    g = pl.program_id(0)
    rb = y_ref.shape[0]
    bs = y_ref.shape[1]
    tiles = y_ref.shape[2] // bs
    for r in range(rb):
        i = g * rb + r
        for tp in range(tiles):
            at = i * tiles + tp
            cols = slice(tp * bs, (tp + 1) * bs)
            stk_ref[cols, 0:bs] = lookup_ref[i0_ref[at]]
            stk_ref[cols, bs:2 * bs] = lookup_ref[i1_ref[at]]
        res = jnp.dot(y_ref[r], stk_ref[...], preferred_element_type=jnp.float32)
        own = self_ref[r].astype(jnp.float32)
        for w in range(2):
            own_w = jnp.where(own_ref[2 * i + w] != 0, own, 0.0)
            out_ref[r, w] = (1.5 * own_w - 0.5 * res[:, w * bs:(w + 1) * bs]).astype(out_ref.dtype)


def _rows_product(i0, i1, own, left, own_blocks, lookup, out_width):
    block_rows, block_size, width = left.shape
    tiles = width // block_size
    nb = lookup.shape[0]
    rb = ROWS_PER_STEP if block_rows % ROWS_PER_STEP == 0 else 1
    return pl.pallas_call(
        _row_kernel,
        out_shape=jax.ShapeDtypeStruct((block_rows, out_width, block_size, block_size), jnp.bfloat16),
        grid_spec=pltpu.PrefetchScalarGridSpec(
            num_scalar_prefetch=3,
            grid=(block_rows // rb,),
            in_specs=[
                pl.BlockSpec((rb, block_size, width), lambda g, *_: (g, 0, 0)),
                pl.BlockSpec((rb, block_size, block_size), lambda g, *_: (g, 0, 0)),
                pl.BlockSpec((nb, block_size, block_size), lambda g, *_: (0, 0, 0)),
            ],
            out_specs=pl.BlockSpec((rb, out_width, block_size, block_size), lambda g, *_: (g, 0, 0, 0)),
            scratch_shapes=[
                pltpu.VMEM((tiles * block_size, out_width * block_size), jnp.bfloat16),
            ],
        ),
        compiler_params=pltpu.CompilerParams(
            dimension_semantics=("arbitrary",),
            vmem_limit_bytes=48 * 1024 * 1024,
        ),
    )(i0, i1, own, left, own_blocks, lookup)


def shards(y_blocks, y_cols, prod_blocks, prod_cols, out_cols):
    block_rows = y_blocks.shape[0]
    block_size = y_blocks.shape[2]
    out_width = out_cols.shape[2]

    groups = lax.axis_size("rows")
    me = lax.axis_index("rows")
    pieces = [prod_blocks[:, 0]]
    for s in range(1, groups):
        pieces.append(lax.ppermute(prod_blocks[:, 0], "rows", [(r, (r + s) % groups) for r in range(groups)]))
    pieces.append(jnp.zeros((1, block_size, block_size), prod_blocks.dtype))
    lookup = jnp.concatenate(pieces, axis=0)
    nb = groups * block_rows
    lookup_cols = lax.all_gather(prod_cols[:, 0], "rows", axis=0, tiled=True)
    left_cols = lax.all_gather(y_cols[:, 0], ("cols", "layers"), axis=0, tiled=False).T

    right_cols = lookup_cols[left_cols]
    owner = left_cols // block_rows
    krow = ((me - owner) % groups) * block_rows + left_cols % block_rows
    i0 = jnp.where(right_cols == out_cols[:, 0, 0][:, None], krow, nb).astype(jnp.int32)
    i1 = jnp.where(right_cols == out_cols[:, 0, 1][:, None], krow, nb).astype(jnp.int32)
    own = (out_cols[:, 0, :] == y_cols[:, 0][:, None]).astype(jnp.int32)

    left = lax.all_gather(y_blocks[:, 0], ("cols", "layers"), axis=2, tiled=True)
    out = _rows_product(
        i0.reshape(-1), i1.reshape(-1), own.reshape(-1), left, y_blocks[:, 0], lookup, out_width)
    return out[:, None]


def solution(mesh):
    placed = (
        P("rows", ("cols", "layers"), None, None),
        P("rows", ("cols", "layers")),
        P("rows", ("cols", "layers"), None, None),
        P("rows", ("cols", "layers")),
        P("rows", ("cols", "layers"), None),
    )
    return jax.shard_map(
        shards,
        mesh=mesh,
        in_specs=placed,
        out_specs=P("rows", ("cols", "layers"), None, None, None),
        check_vma=False,
    )
```

```python
import jax
import jax.numpy as jnp
from jax import lax
from jax.experimental import pallas as pl
from jax.experimental.pallas import tpu as pltpu
from jax.sharding import PartitionSpec as P


def _stack_kernel(krow_ref, lookup_ref, out_ref):
    i = pl.program_id(0)
    tiles = out_ref.shape[1] // out_ref.shape[2]
    bs = out_ref.shape[2]
    for tp in range(tiles):
        out_ref[0, tp * bs:(tp + 1) * bs, :] = lookup_ref[krow_ref[i * tiles + tp]]


def _stack_rows(krow, lookup, block_rows, tiles):
    nb, bs, _ = lookup.shape
    return pl.pallas_call(
        _stack_kernel,
        out_shape=jax.ShapeDtypeStruct((block_rows, tiles * bs, bs), lookup.dtype),
        grid_spec=pltpu.PrefetchScalarGridSpec(
            num_scalar_prefetch=1,
            grid=(block_rows,),
            in_specs=[pl.BlockSpec((nb, bs, bs), lambda i, *_: (0, 0, 0))],
            out_specs=pl.BlockSpec((1, tiles * bs, bs), lambda i, *_: (i, 0, 0)),
        ),
        compiler_params=pltpu.CompilerParams(
            dimension_semantics=("arbitrary",),
            vmem_limit_bytes=40 * 1024 * 1024,
        ),
    )(krow, lookup)


ROWS_PER_STEP = 4


def _row_kernel(m0_ref, m1_ref, own_ref, y_ref, self_ref, stk_ref, out_ref, lhs_ref):
    g = pl.program_id(0)
    tiles = y_ref.shape[0]
    rb = y_ref.shape[1]
    bs = y_ref.shape[-1]
    for r in range(rb):
        i = g * rb + r
        for tp in range(tiles):
            at = i * tiles + tp
            cols = slice(tp * bs, (tp + 1) * bs)
            y = y_ref[tp, r]
            zero = jnp.zeros_like(y)
            lhs_ref[0:bs, cols] = jnp.where(m0_ref[at] != 0, y, zero)
            lhs_ref[bs:2 * bs, cols] = jnp.where(m1_ref[at] != 0, y, zero)
        res = jnp.dot(lhs_ref[...], stk_ref[r], preferred_element_type=jnp.float32)
        own = self_ref[r].astype(jnp.float32)
        for w in range(2):
            own_w = jnp.where(own_ref[2 * i + w] != 0, own, 0.0)
            out_ref[r, w] = (1.5 * own_w - 0.5 * res[w * bs:(w + 1) * bs]).astype(out_ref.dtype)


def _rows_product(m0, m1, own, left, own_blocks, stacked, out_width):
    tiles, block_rows, block_size, _ = left.shape
    rb = ROWS_PER_STEP if block_rows % ROWS_PER_STEP == 0 else 1
    return pl.pallas_call(
        _row_kernel,
        out_shape=jax.ShapeDtypeStruct((block_rows, out_width, block_size, block_size), jnp.bfloat16),
        grid_spec=pltpu.PrefetchScalarGridSpec(
            num_scalar_prefetch=3,
            grid=(block_rows // rb,),
            in_specs=[
                pl.BlockSpec((tiles, rb, block_size, block_size), lambda g, *_: (0, g, 0, 0)),
                pl.BlockSpec((rb, block_size, block_size), lambda g, *_: (g, 0, 0)),
                pl.BlockSpec((rb, tiles * block_size, block_size), lambda g, *_: (g, 0, 0)),
            ],
            out_specs=pl.BlockSpec((rb, out_width, block_size, block_size), lambda g, *_: (g, 0, 0, 0)),
            scratch_shapes=[
                pltpu.VMEM((out_width * block_size, tiles * block_size), jnp.bfloat16),
            ],
        ),
        compiler_params=pltpu.CompilerParams(
            dimension_semantics=("arbitrary",),
            vmem_limit_bytes=48 * 1024 * 1024,
        ),
    )(m0, m1, own, left, own_blocks, stacked)


def shards(y_blocks, y_cols, prod_blocks, prod_cols, out_cols):
    block_rows = y_blocks.shape[0]
    block_size = y_blocks.shape[2]
    out_width = out_cols.shape[2]

    groups = lax.axis_size("rows")
    me = lax.axis_index("rows")
    pieces = [prod_blocks[:, 0]]
    for s in range(1, groups):
        pieces.append(lax.ppermute(prod_blocks[:, 0], "rows", [(r, (r + s) % groups) for r in range(groups)]))
    lookup = jnp.concatenate(pieces, axis=0)
    lookup_cols = lax.all_gather(prod_cols[:, 0], "rows", axis=0, tiled=True)
    left_cols = lax.all_gather(y_cols[:, 0], ("cols", "layers"), axis=0, tiled=False).T

    right_cols = lookup_cols[left_cols]
    owner = left_cols // block_rows
    krow = ((me - owner) % groups) * block_rows + left_cols % block_rows
    m0 = (right_cols == out_cols[:, 0, 0][:, None]).astype(jnp.int32)
    m1 = (right_cols == out_cols[:, 0, 1][:, None]).astype(jnp.int32)
    own = (out_cols[:, 0, :] == y_cols[:, 0][:, None]).astype(jnp.int32)

    tiles = left_cols.shape[1]
    stacked = _stack_rows(krow.reshape(-1).astype(jnp.int32), lookup, block_rows, tiles)

    left = lax.all_gather(y_blocks[:, 0], ("cols", "layers"), axis=0, tiled=False)
    out = _rows_product(m0.reshape(-1), m1.reshape(-1), own.reshape(-1), left, y_blocks[:, 0], stacked, out_width)
    return out[:, None]


def solution(mesh):
    placed = (
        P("rows", ("cols", "layers"), None, None),
        P("rows", ("cols", "layers")),
        P("rows", ("cols", "layers"), None, None),
        P("rows", ("cols", "layers")),
        P("rows", ("cols", "layers"), None),
    )
    return jax.shard_map(
        shards,
        mesh=mesh,
        in_specs=placed,
        out_specs=P("rows", ("cols", "layers"), None, None, None),
        check_vma=False,
    )
```

```python
import jax
import jax.numpy as jnp
from jax import lax
from jax.experimental import pallas as pl
from jax.experimental.pallas import tpu as pltpu
from jax.sharding import PartitionSpec as P


ROWS_PER_STEP = 3


def _row_kernel(i0_ref, i1_ref, own_ref, y_ref, self_ref, lookup_ref, out_ref, lhs_ref, stk_ref):
    g = pl.program_id(0)
    tiles = y_ref.shape[0]
    rb = y_ref.shape[1]
    bs = y_ref.shape[-1]
    for r in range(rb):
        i = g * rb + r
        for tp in range(tiles):
            at = i * tiles + tp
            cols = slice(tp * bs, (tp + 1) * bs)
            lhs_ref[:, cols] = y_ref[tp, r]
            stk_ref[cols, 0:bs] = lookup_ref[i0_ref[at]]
            stk_ref[cols, bs:2 * bs] = lookup_ref[i1_ref[at]]
        res = jnp.dot(lhs_ref[...], stk_ref[...], preferred_element_type=jnp.float32)
        own = self_ref[r].astype(jnp.float32)
        for w in range(2):
            own_w = jnp.where(own_ref[2 * i + w] != 0, own, 0.0)
            out_ref[r, w] = (1.5 * own_w - 0.5 * res[:, w * bs:(w + 1) * bs]).astype(out_ref.dtype)


def _rows_product(i0, i1, own, left, own_blocks, lookup, out_width):
    tiles, block_rows, block_size, _ = left.shape
    nb = lookup.shape[0]
    rb = ROWS_PER_STEP if block_rows % ROWS_PER_STEP == 0 else 1
    return pl.pallas_call(
        _row_kernel,
        out_shape=jax.ShapeDtypeStruct((block_rows, out_width, block_size, block_size), jnp.bfloat16),
        grid_spec=pltpu.PrefetchScalarGridSpec(
            num_scalar_prefetch=3,
            grid=(block_rows // rb,),
            in_specs=[
                pl.BlockSpec((tiles, rb, block_size, block_size), lambda g, *_: (0, g, 0, 0)),
                pl.BlockSpec((rb, block_size, block_size), lambda g, *_: (g, 0, 0)),
                pl.BlockSpec((nb, block_size, block_size), lambda g, *_: (0, 0, 0)),
            ],
            out_specs=pl.BlockSpec((rb, out_width, block_size, block_size), lambda g, *_: (g, 0, 0, 0)),
            scratch_shapes=[
                pltpu.VMEM((block_size, tiles * block_size), jnp.bfloat16),
                pltpu.VMEM((tiles * block_size, out_width * block_size), jnp.bfloat16),
            ],
        ),
        compiler_params=pltpu.CompilerParams(
            dimension_semantics=("arbitrary",),
            vmem_limit_bytes=48 * 1024 * 1024,
        ),
    )(i0, i1, own, left, own_blocks, lookup)


def shards(y_blocks, y_cols, prod_blocks, prod_cols, out_cols):
    block_rows = y_blocks.shape[0]
    block_size = y_blocks.shape[2]
    out_width = out_cols.shape[2]

    groups = lax.axis_size("rows")
    me = lax.axis_index("rows")
    pieces = [prod_blocks[:, 0]]
    for s in range(1, groups):
        pieces.append(lax.ppermute(prod_blocks[:, 0], "rows", [(r, (r + s) % groups) for r in range(groups)]))
    pieces.append(jnp.zeros((1, block_size, block_size), prod_blocks.dtype))
    lookup = jnp.concatenate(pieces, axis=0)
    nb = groups * block_rows
    lookup_cols = lax.all_gather(prod_cols[:, 0], "rows", axis=0, tiled=True)
    left_cols = lax.all_gather(y_cols[:, 0], ("cols", "layers"), axis=0, tiled=False).T

    right_cols = lookup_cols[left_cols]
    owner = left_cols // block_rows
    krow = ((me - owner) % groups) * block_rows + left_cols % block_rows
    i0 = jnp.where(right_cols == out_cols[:, 0, 0][:, None], krow, nb).astype(jnp.int32)
    i1 = jnp.where(right_cols == out_cols[:, 0, 1][:, None], krow, nb).astype(jnp.int32)
    own = (out_cols[:, 0, :] == y_cols[:, 0][:, None]).astype(jnp.int32)

    left = lax.all_gather(y_blocks[:, 0], ("cols", "layers"), axis=0, tiled=False)
    out = _rows_product(
        i0.reshape(-1), i1.reshape(-1), own.reshape(-1), left, y_blocks[:, 0], lookup, out_width)
    return out[:, None]


def solution(mesh):
    placed = (
        P("rows", ("cols", "layers"), None, None),
        P("rows", ("cols", "layers")),
        P("rows", ("cols", "layers"), None, None),
        P("rows", ("cols", "layers")),
        P("rows", ("cols", "layers"), None),
    )
    return jax.shard_map(
        shards,
        mesh=mesh,
        in_specs=placed,
        out_specs=P("rows", ("cols", "layers"), None, None, None),
        check_vma=False,
    )
```

```python
import jax
import jax.numpy as jnp
from jax import lax
from jax.experimental import pallas as pl
from jax.experimental.pallas import tpu as pltpu
from jax.sharding import PartitionSpec as P


ROWS_PER_STEP = 4


def _row_kernel(i0_ref, i1_ref, own_ref, y_ref, self_ref, lookup_ref, out_ref, lhs_ref, stk_ref, sems):
    g = pl.program_id(0)
    tiles = y_ref.shape[0]
    rb = y_ref.shape[1]
    bs = y_ref.shape[-1]
    for r in range(rb):
        i = g * rb + r
        copies = []
        for tp in range(tiles):
            copy = pltpu.make_async_copy(y_ref.at[tp, r], lhs_ref.at[:, pl.ds(tp * bs, bs)], sems.at[tp])
            copy.start()
            copies.append(copy)
        for tp in range(tiles):
            at = i * tiles + tp
            cols = slice(tp * bs, (tp + 1) * bs)
            stk_ref[cols, 0:bs] = lookup_ref[i0_ref[at]]
            stk_ref[cols, bs:2 * bs] = lookup_ref[i1_ref[at]]
        for copy in copies:
            copy.wait()
        res = jnp.dot(lhs_ref[...], stk_ref[...], preferred_element_type=jnp.float32)
        own = self_ref[r].astype(jnp.float32)
        for w in range(2):
            own_w = jnp.where(own_ref[2 * i + w] != 0, own, 0.0)
            out_ref[r, w] = (1.5 * own_w - 0.5 * res[:, w * bs:(w + 1) * bs]).astype(out_ref.dtype)


def _rows_product(i0, i1, own, left, own_blocks, lookup, out_width):
    tiles, block_rows, block_size, _ = left.shape
    nb = lookup.shape[0]
    rb = ROWS_PER_STEP if block_rows % ROWS_PER_STEP == 0 else 1
    return pl.pallas_call(
        _row_kernel,
        out_shape=jax.ShapeDtypeStruct((block_rows, out_width, block_size, block_size), jnp.bfloat16),
        grid_spec=pltpu.PrefetchScalarGridSpec(
            num_scalar_prefetch=3,
            grid=(block_rows // rb,),
            in_specs=[
                pl.BlockSpec((tiles, rb, block_size, block_size), lambda g, *_: (0, g, 0, 0)),
                pl.BlockSpec((rb, block_size, block_size), lambda g, *_: (g, 0, 0)),
                pl.BlockSpec((nb, block_size, block_size), lambda g, *_: (0, 0, 0)),
            ],
            out_specs=pl.BlockSpec((rb, out_width, block_size, block_size), lambda g, *_: (g, 0, 0, 0)),
            scratch_shapes=[
                pltpu.VMEM((block_size, tiles * block_size), jnp.bfloat16),
                pltpu.VMEM((tiles * block_size, out_width * block_size), jnp.bfloat16),
                pltpu.SemaphoreType.DMA((tiles,)),
            ],
        ),
        compiler_params=pltpu.CompilerParams(
            dimension_semantics=("arbitrary",),
            vmem_limit_bytes=48 * 1024 * 1024,
        ),
    )(i0, i1, own, left, own_blocks, lookup)


def shards(y_blocks, y_cols, prod_blocks, prod_cols, out_cols):
    block_rows = y_blocks.shape[0]
    block_size = y_blocks.shape[2]
    out_width = out_cols.shape[2]

    groups = lax.axis_size("rows")
    me = lax.axis_index("rows")
    pieces = [prod_blocks[:, 0]]
    for s in range(1, groups):
        pieces.append(lax.ppermute(prod_blocks[:, 0], "rows", [(r, (r + s) % groups) for r in range(groups)]))
    pieces.append(jnp.zeros((1, block_size, block_size), prod_blocks.dtype))
    lookup = jnp.concatenate(pieces, axis=0)
    nb = groups * block_rows
    lookup_cols = lax.all_gather(prod_cols[:, 0], "rows", axis=0, tiled=True)
    left_cols = lax.all_gather(y_cols[:, 0], ("cols", "layers"), axis=0, tiled=False).T

    right_cols = lookup_cols[left_cols]
    owner = left_cols // block_rows
    krow = ((me - owner) % groups) * block_rows + left_cols % block_rows
    i0 = jnp.where(right_cols == out_cols[:, 0, 0][:, None], krow, nb).astype(jnp.int32)
    i1 = jnp.where(right_cols == out_cols[:, 0, 1][:, None], krow, nb).astype(jnp.int32)
    own = (out_cols[:, 0, :] == y_cols[:, 0][:, None]).astype(jnp.int32)

    left = lax.all_gather(y_blocks[:, 0], ("cols", "layers"), axis=0, tiled=False)
    out = _rows_product(
        i0.reshape(-1), i1.reshape(-1), own.reshape(-1), left, y_blocks[:, 0], lookup, out_width)
    return out[:, None]


def solution(mesh):
    placed = (
        P("rows", ("cols", "layers"), None, None),
        P("rows", ("cols", "layers")),
        P("rows", ("cols", "layers"), None, None),
        P("rows", ("cols", "layers")),
        P("rows", ("cols", "layers"), None),
    )
    return jax.shard_map(
        shards,
        mesh=mesh,
        in_specs=placed,
        out_specs=P("rows", ("cols", "layers"), None, None, None),
        check_vma=False,
    )
```
